256 devices in a mesh: col: 32 (over z, x), sub: 8 (over y, core).
Axes of the slice: x: 4, y: 4, z: 8, core: 2. Of those that a mesh axis runs over, the one named last changes fastest.
Arguments:
- slab: float32 [512, 16, 65536], P(None, 'sub', 'col'), may hold values from -120 to 120
- start_basis: float32 [512, 128], replicated, may hold values from -6 to 6
Outputs:
- core_tensor: float32 [128, 16, 65536], P('col', 'sub')
The draws below stay inside these ranges and needn't reach their ends.
All inputs are finite; a program needn't handle non-finite values.
Results may differ from the reference program's by a relative error of at most 0.0003.
Values sent between devices are 32-bit elements; how exact they have to be, the bound alone decides.
No kernel may reach another device: no remote copies, remote signals or barrier semaphores. Data moves between devices by JAX's collectives and lax.ppermute only.
A program may use at most 128 MiB of HBM per device.

```python
import math
import jax
import jax.numpy as jnp
from jax import lax

RUNS = 512
RANK = 128
STEPS = 16
ITERS = 2
CELLS = 65536


def draw_slab(key, part):
    keys = jax.random.split(jax.random.fold_in(key, 11), 3)
    log_rows = jax.random.uniform(keys[1], (RUNS, 1, 1), jnp.float32, 0.0, math.log(3.0))
    col_factor = jnp.exp(jax.random.uniform(keys[2], (1, STEPS, CELLS), jnp.float32, math.log(0.3), math.log(3.0)))
    step_pos = jnp.arange(STEPS, dtype=jnp.float32).reshape(1, STEPS, 1) / STEPS
    cell_pos = jnp.arange(CELLS, dtype=jnp.float32).reshape(1, 1, CELLS) / CELLS
    ramp = jnp.exp((step_pos + cell_pos - 1.0) * math.log(3.0))
    base = jax.random.truncated_normal(keys[0], -4.0, 4.0, (RUNS, STEPS, CELLS), jnp.float32)
    values = base * jnp.exp(log_rows) * col_factor * ramp
    return values.astype(jnp.float32)


def normal_values(key, shape, scale, most, held_as=jnp.bfloat16):
    result = jax.random.normal(key, shape, jnp.float32) * scale
    return jnp.minimum(jnp.maximum(result, -most), most).astype(held_as)


def setup_inputs(seed: int = 0) -> dict:
    streams_of = jax.random.split(jax.random.key(seed), 3)
    slab = draw_slab(jax.random.fold_in(streams_of[2], 71), 0)
    start_basis = normal_values(streams_of[1], (RUNS, RANK), 1.0, 6.0, jnp.float32)
    return dict(slab=slab, start_basis=start_basis)


def refine(gram, basis):
    for step in range(ITERS):
        image = jnp.dot(gram.astype(jnp.float32), basis.astype(jnp.float32), precision=lax.Precision.HIGHEST, preferred_element_type=jnp.float32)
        inner = jnp.dot(image.T.astype(jnp.float32), image.astype(jnp.float32), precision=lax.Precision.HIGHEST, preferred_element_type=jnp.float32)
        factor = jnp.linalg.cholesky(inner)
        basis = lax.linalg.triangular_solve(factor, image, left_side=False, lower=True, transpose_a=True)
    return basis

def reference(slab, start_basis):
    unfolded = slab.reshape(RUNS, STEPS * CELLS)
    gram = jnp.dot(unfolded.astype(jnp.float32), unfolded.T.astype(jnp.float32), precision=lax.Precision.HIGHEST, preferred_element_type=jnp.float32)
    basis = refine(gram, start_basis)
    core = jnp.dot(basis.T.astype(jnp.float32), unfolded.astype(jnp.float32), precision=lax.Precision.HIGHEST, preferred_element_type=jnp.float32)
    return core.reshape(RANK, STEPS, CELLS)
```

```python
import functools

import jax
import jax.numpy as jnp
from jax import lax
from jax.sharding import PartitionSpec as P

ITERS = 2


def orthonormal(image):
    inner = jnp.dot(
        image.T, image, precision=lax.Precision.HIGHEST, preferred_element_type=jnp.float32
    )
    factor = jnp.linalg.cholesky(inner)
    return lax.linalg.triangular_solve(factor, image, left_side=False, lower=True, transpose_a=True)


def refine(gram, basis, passes):
    for step in range(passes):
        image = jnp.dot(
            gram, basis, precision=lax.Precision.HIGHEST, preferred_element_type=jnp.float32
        )
        basis = orthonormal(image)
    return basis


def exchange_sum(value, names, size):
    bits = size.bit_length() - 1
    if size != 1 << bits or value.shape[0] % size:
        return lax.psum(value, names)
    index = lax.axis_index(names)
    for bit in range(bits):
        half = value.shape[0] // 2
        upper = (index >> bit) & 1
        low, high = value[:half], value[half:]
        keep = jnp.where(upper == 1, high, low)
        send = jnp.where(upper == 1, low, high)
        pairs = [(i, i ^ (1 << bit)) for i in range(size)]
        value = keep + lax.ppermute(send, names, pairs)
    for bit in reversed(range(bits)):
        upper = (index >> bit) & 1
        pairs = [(i, i ^ (1 << bit)) for i in range(size)]
        other = lax.ppermute(value, names, pairs)
        value = jnp.where(
            upper == 1, jnp.concatenate([other, value]), jnp.concatenate([value, other])
        )
    return value


def local(slab, start_basis, size):
    run_count, step_local, cell_local = slab.shape
    unfolded = slab.reshape(run_count, step_local * cell_local)
    local_gram = jnp.dot(
        unfolded, unfolded.T, precision=lax.Precision.HIGHEST, preferred_element_type=jnp.float32
    )
    gram = exchange_sum(local_gram, ("col", "sub"), size)
    basis = refine(gram, start_basis, ITERS)
    projected = jnp.dot(
        basis.T, unfolded, precision=lax.Precision.HIGHEST, preferred_element_type=jnp.float32
    )
    projected = projected.reshape(basis.shape[1], step_local, cell_local)
    return lax.all_to_all(projected, "col", split_axis=0, concat_axis=2, tiled=True)


def solution(mesh):
    size = mesh.shape["col"] * mesh.shape["sub"]
    return jax.shard_map(
        functools.partial(local, size=size),
        mesh=mesh,
        in_specs=(P(None, "sub", "col"), P()),
        out_specs=P("col", "sub", None),
        check_vma=False,
    )
```

```python
import functools

import jax
import jax.numpy as jnp
from jax import lax
from jax.sharding import PartitionSpec as P

ITERS = 2


def orthonormal(image):
    inner = jnp.dot(
        image.T, image, precision=lax.Precision.HIGHEST, preferred_element_type=jnp.float32
    )
    factor = jnp.linalg.cholesky(inner)
    return lax.linalg.triangular_solve(factor, image, left_side=False, lower=True, transpose_a=True)


def refine(gram, basis, passes):
    for step in range(passes):
        image = jnp.dot(
            gram, basis, precision=lax.Precision.HIGHEST, preferred_element_type=jnp.float32
        )
        basis = orthonormal(image)
    return basis


def exchange_sum(value, names, size):
    bits = size.bit_length() - 1
    if size != 1 << bits or value.shape[0] % size:
        return lax.psum(value, names)
    index = lax.axis_index(names)
    for bit in range(bits):
        half = value.shape[0] // 2
        upper = (index >> bit) & 1
        low, high = value[:half], value[half:]
        keep = jnp.where(upper == 1, high, low)
        send = jnp.where(upper == 1, low, high)
        pairs = [(i, i ^ (1 << bit)) for i in range(size)]
        value = keep + lax.ppermute(send, names, pairs)
    for bit in reversed(range(bits)):
        upper = (index >> bit) & 1
        pairs = [(i, i ^ (1 << bit)) for i in range(size)]
        other = lax.ppermute(value, names, pairs)
        value = jnp.where(
            upper == 1, jnp.concatenate([other, value]), jnp.concatenate([value, other])
        )
    return value


def local(slab, start_basis, size):
    run_count, step_local, cell_local = slab.shape
    unfolded = slab.reshape(run_count, step_local * cell_local)
    local_gram = jnp.dot(
        unfolded, unfolded.T, precision=lax.Precision.HIGHEST, preferred_element_type=jnp.float32
    )
    gram = exchange_sum(local_gram, ("col", "sub"), size)
    basis = refine(gram, start_basis, ITERS)
    projected = jnp.einsum(
        "rk,rsc->ksc", basis, slab, precision=lax.Precision.HIGHEST, preferred_element_type=jnp.float32
    )
    return lax.all_to_all(projected, "col", split_axis=0, concat_axis=2, tiled=True)


def solution(mesh):
    size = mesh.shape["col"] * mesh.shape["sub"]
    return jax.shard_map(
        functools.partial(local, size=size),
        mesh=mesh,
        in_specs=(P(None, "sub", "col"), P()),
        out_specs=P("col", "sub", None),
        check_vma=False,
    )
```
